512 devices in a mesh: sub: 128 (over y, z, core), case: 4 (over x).
Axes of the slice: x: 4, y: 4, z: 16, core: 2. Of those that a mesh axis runs over, the one named last changes fastest.
Arguments:
- load_interior: float32 [128, 128, 4096], P('sub', None, 'case'), may hold values from -6 to 6
- load_boundary: float32 [128, 128, 1024], P('sub', None, 'case'), may hold values from -6 to 6
- cond_blocks: float32 [128, 128, 4096], P('sub', 'case'), may hold values from -0.25 to 0.25
- block_rows: int32 [128, 128], P('sub', 'case'), may hold values from 0 to 15
- block_cols: int32 [128, 128], P('sub', 'case'), may hold values from 0 to 63, as said below
- interface_maps: int32 [128, 7, 2, 1024], P('sub'), may hold values from 0 to 1023, as said below
- merge_maps: float32 [128, 7, 1024, 512], P('sub', None, 'case'), as said below
Outputs:
- leaf_loads: float32 [128, 1024, 128], P('sub', 'case')
- node_loads: float32 [128, 1024, 128], P('sub', 'case')
The draws below stay inside these ranges and needn't reach their ends.
Inputs may be any that keep to these rules, and one draw needn't show every extreme that they name: `block_cols`: entry k of a substructure's row lies in [(k // 32) * 16, (k // 32 + 1) * 16); blocks may repeat. `interface_maps`: each row of 1024 entries is a permutation; at level index l, slots that agree in all but their lowest l + 1 bits hold equal entries. `merge_maps`: at level index l, slots that agree in all but their lowest l + 1 bits hold equal entries.
All inputs are finite; a program needn't handle non-finite values.
Results may differ from the reference program's by a relative error of at most 0.0003.
Values sent between devices are 32-bit elements; how exact they have to be, the bound alone decides.
No kernel may reach another device: no remote copies, remote signals or barrier semaphores. Data moves between devices by JAX's collectives and lax.ppermute only.
A program may use at most 64 MiB of HBM per device.

```python
import jax
import jax.numpy as jnp
from jax import lax

NIF = 1024
NS = 512
NI = 4096
BLK = 64
NNZD = 32
CASES = 128
SUBS = 128
NNZ = 128
NBL = 16
NBR = 16
LEVELS = 7


def draw_block_cols(key, part):
    owner = jnp.arange(NNZ, dtype=jnp.int32) // NNZD
    offset = jax.random.randint(key, (SUBS, NNZ), 0, NBL, dtype=jnp.int32)
    return owner[None, :] * NBL + offset


def draw_interface_maps(key, part):
    levels_list = []
    for level in range(1, LEVELS + 1):
        count = SUBS // 2 ** level
        keys = jax.random.split(jax.random.fold_in(key, 100 + level), count * 2)
        perms = jax.vmap(lambda k: jax.random.permutation(k, NIF))(keys).astype(jnp.int32)
        perms = perms.reshape(count, 2, NIF)
        levels_list.append(jnp.repeat(perms, 2 ** level, axis=0))
    return jnp.stack(levels_list, axis=1)


def draw_merge_maps(key, part):
    levels_list = []
    for level in range(1, LEVELS + 1):
        count = SUBS // 2 ** level
        values = jax.random.normal(jax.random.fold_in(key, 200 + level), (count, NIF, NS), jnp.float32)
        values = values * (4.0 * NS) ** (-0.5)
        levels_list.append(jnp.repeat(values, 2 ** level, axis=0))
    return jnp.stack(levels_list, axis=1)


def touch_ends(entries, own_key, low, largest):
    dims = entries.shape
    index_at = [jax.random.randint(jax.random.fold_in(own_key, axis), (), 0, dims[axis]) for axis in range(len(dims))]
    entries = entries.at[tuple(index_at)].set(low)
    longest = dims.index(max(dims))
    index_at[longest] = (index_at[longest] + 1) % dims[longest]
    return entries.at[tuple(index_at)].set(largest)


def block_scale(stream_key, shape, cuts, smallest, high):
    factor_of = 1.0
    for position, shards_of in cuts:
        steps = jax.random.uniform(jax.random.fold_in(jax.random.fold_in(stream_key, 6), position), (shards_of,), jnp.float32, smallest / len(cuts), high / len(cuts))
        factor_of = factor_of * jnp.repeat(jnp.exp(steps), shape[position] // shards_of).reshape((-1,) + (1,) * (len(shape) - 1 - position))
    return factor_of


def noise(own_key, dims, spread, limit, cuts=(), held_as=jnp.bfloat16):
    values = spread * jax.random.normal(own_key, dims, jnp.float32)
    if cuts:
        values = values * block_scale(own_key, dims, cuts, -0.22, 0.18)
    return jnp.clip(values, -limit, limit).astype(held_as)


def setup_inputs(seed: int = 0) -> dict:
    key_of = jax.random.split(jax.random.key(seed), 8)
    load_interior = noise(key_of[0], (CASES, SUBS, NI), 1.0, 6.0, ((0, 128), (2, 4)), jnp.float32)
    load_boundary = noise(key_of[1], (CASES, SUBS, NIF), 1.0, 6.0, ((0, 128), (2, 4)), jnp.float32)
    cond_blocks = noise(key_of[2], (SUBS, NNZ, BLK * BLK), (NNZ * BLK * BLK // NIF) ** -0.5, 0.25, ((0, 128), (1, 4)), jnp.float32)
    block_rows = touch_ends(jax.random.randint(key_of[3], (SUBS, NNZ), 0, NBR), jax.random.fold_in(key_of[3], 1), 0, NBR - 1).astype(jnp.int32)
    block_cols = draw_block_cols(jax.random.fold_in(key_of[7], 71), 0)
    interface_maps = draw_interface_maps(jax.random.fold_in(key_of[7], 71), 0)
    merge_maps = draw_merge_maps(jax.random.fold_in(key_of[7], 71), 0)
    return {"load_interior": load_interior, "load_boundary": load_boundary, "cond_blocks": cond_blocks, "block_rows": block_rows, "block_cols": block_cols, "interface_maps": interface_maps, "merge_maps": merge_maps}


def condense(inputs):
    interior, boundary, blocks, rows, cols = inputs
    pieces = interior.reshape(NI // BLK, BLK, CASES)[cols]
    square = blocks.reshape(NNZ, BLK, BLK)
    products = jnp.einsum("krc,kcn->krn", square, pieces, precision=lax.Precision.HIGHEST)
    onehot = (rows[None, :] == jnp.arange(NBR, dtype=jnp.int32)[:, None]).astype(jnp.float32)
    summed = jnp.dot(onehot, products.reshape(NNZ, BLK * CASES), precision=lax.Precision.HIGHEST)
    return boundary - summed.reshape(NIF, CASES)


def merge_one(left, right, maps, matrix):
    shared = left[maps[0, :NS]] + right[maps[1, :NS]]
    kept = jnp.concatenate([left[maps[0, NS:]], right[maps[1, NS:]]], axis=0)
    return kept - jnp.dot(matrix, shared, precision=lax.Precision.HIGHEST)


def reference(load_interior, load_boundary, cond_blocks, block_rows, block_cols, interface_maps, merge_maps):
    interior_all = jnp.transpose(load_interior, (1, 2, 0))
    boundary_all = jnp.transpose(load_boundary, (1, 2, 0))
    leaves = lax.map(condense, (interior_all, boundary_all, cond_blocks, block_rows, block_cols))
    nodes = jnp.zeros_like(leaves)
    values = leaves
    for level in range(1, LEVELS + 1):
        half = 2 ** (level - 1)
        left = values[0::2]
        right = values[1::2]
        maps = interface_maps[half::2 * half, level - 1]
        mats = merge_maps[half::2 * half, level - 1]
        parents = jax.vmap(merge_one)(left, right, maps, mats)
        nodes = nodes.at[half::2 * half].set(parents)
        values = parents
    nodes = nodes.at[0].set(values[0])
    return leaves, nodes
```

```python
import jax
import jax.numpy as jnp
from jax import lax
from jax.sharding import PartitionSpec as P

BLK = 64


def from_partner(value, axis, distance):
    mask = 2**distance
    pairs = [(source, source ^ mask) for source in range(lax.axis_size(axis))]
    return lax.ppermute(value, axis, pairs)


def shifted(value, axis, shift):
    size = lax.axis_size(axis)
    pairs = [(source, (source + shift) % size) for source in range(size)]
    return lax.ppermute(value, axis, pairs)


def case_allreduce(value, position):
    groups = lax.axis_size("case")
    quarter = value.shape[0] // groups
    chunks = value.reshape(groups, quarter, value.shape[1])
    mine = chunks[position]
    for shift in range(1, groups):
        outgoing = chunks[(position + shift) % groups]
        mine = mine + shifted(outgoing, "case", shift)
    pieces = [mine] + [shifted(mine, "case", shift) for shift in range(1, groups)]
    stacked = jnp.stack(pieces)
    order = (position - jnp.arange(groups)) % groups
    full = jnp.take(stacked, order, axis=0).reshape(value.shape)
    return mine, full


def on_device(
    load_interior, load_boundary, cond_blocks, block_rows, block_cols, interface_maps, merge_maps
):
    local_rows = load_interior.shape[2]
    quarter = load_boundary.shape[2]
    joined = jnp.concatenate([load_interior, load_boundary], axis=2)
    joined = lax.all_to_all(joined, "sub", split_axis=1, concat_axis=0, tiled=True)
    interior = jnp.transpose(joined[:, 0, :local_rows])
    boundary = jnp.transpose(joined[:, 0, local_rows:])
    num_cases = interior.shape[1]
    block_count = cond_blocks.shape[1]
    block_size = BLK
    blocks = cond_blocks[0].reshape(block_count, block_size, block_size)
    groups = lax.axis_size("case")
    full_rows = quarter * groups
    position = lax.axis_index("case")
    local_cols = block_cols[0] - position * (local_rows // block_size)
    pieces = jnp.take(
        interior.reshape(local_rows // block_size, block_size, num_cases), local_cols, axis=0
    )
    products = jnp.einsum("krc,kcn->krn", blocks, pieces, precision=lax.Precision.HIGHEST)
    row_blocks = full_rows // block_size
    onehot = (block_rows[0][None, :] == jnp.arange(row_blocks, dtype=jnp.int32)[:, None]).astype(
        jnp.float32
    )
    partial_value = jnp.dot(
        onehot,
        products.reshape(block_count, block_size * num_cases),
        precision=lax.Precision.HIGHEST,
    )
    partial_value = partial_value.reshape(full_rows, num_cases)
    embedded = lax.dynamic_update_slice(
        jnp.zeros((full_rows, num_cases), jnp.float32), boundary, (position * quarter, 0)
    )
    contribution = embedded - partial_value
    leaf_share, current = case_allreduce(contribution, position)
    slot = lax.axis_index("sub")
    levels = lax.axis_size("sub").bit_length() - 1
    nodes = jnp.zeros((quarter, num_cases), jnp.float32)
    for level in range(1, levels + 1):
        half = 1 << level - 1
        maps = interface_maps[0, level - 1]
        last = level == levels
        if last:
            matrix = merge_maps[0, level - 1]
        else:
            matrix = lax.all_gather(merge_maps[0, level - 1], "case", axis=0, tiled=True)
        shared_rows = matrix.shape[1]
        other = from_partner(current, "sub", level - 1)
        upper = slot // half % 2 == 1
        left_base = jnp.where(upper, full_rows, 0)
        right_base = full_rows - left_base
        stacked = jnp.concatenate([current, other], axis=0)
        shared = jnp.take(stacked, maps[0, :shared_rows] + left_base, axis=0) + jnp.take(
            stacked, maps[1, :shared_rows] + right_base, axis=0
        )
        kept_index = jnp.concatenate(
            [maps[0, shared_rows:] + left_base, maps[1, shared_rows:] + right_base]
        )
        if last:
            kept_index = lax.dynamic_slice_in_dim(kept_index, position * quarter, quarter)
        parent = jnp.take(stacked, kept_index, axis=0) - jnp.dot(
            matrix, shared, precision=lax.Precision.HIGHEST
        )
        is_node = slot % (2 * half) == half
        if last:
            is_node = jnp.logical_or(is_node, slot == 0)
            own = parent
        else:
            own = lax.dynamic_slice_in_dim(parent, position * quarter, quarter, 0)
        nodes = jnp.where(is_node, own, nodes)
        current = parent
    return (leaf_share[None], nodes[None])


def solution(mesh):
    placed = (
        P("sub", None, "case"),
        P("sub", None, "case"),
        P("sub", "case", None),
        P("sub", "case"),
        P("sub", "case"),
        P("sub", None, None, None),
        P("sub", None, "case", None),
    )
    return jax.shard_map(
        on_device,
        mesh=mesh,
        in_specs=placed,
        out_specs=(P("sub", "case", None), P("sub", "case", None)),
        check_vma=False,
    )
```

```python
import jax
import jax.numpy as jnp
from jax import lax
from jax.sharding import PartitionSpec as P

BLK = 64


def from_partner(value, axis, distance):
    mask = 2**distance
    pairs = [(source, source ^ mask) for source in range(lax.axis_size(axis))]
    return lax.ppermute(value, axis, pairs)


def shifted(value, axis, shift):
    size = lax.axis_size(axis)
    pairs = [(source, (source + shift) % size) for source in range(size)]
    return lax.ppermute(value, axis, pairs)


def case_allreduce(value, position):
    groups = lax.axis_size("case")
    quarter = value.shape[0] // groups
    chunks = value.reshape(groups, quarter, value.shape[1])
    mine = chunks[position]
    for shift in range(1, groups):
        outgoing = chunks[(position + shift) % groups]
        mine = mine + shifted(outgoing, "case", shift)
    pieces = [mine] + [shifted(mine, "case", shift) for shift in range(1, groups)]
    stacked = jnp.stack(pieces)
    order = (position - jnp.arange(groups)) % groups
    full = jnp.take(stacked, order, axis=0).reshape(value.shape)
    return mine, full


def on_device(
    load_interior, load_boundary, cond_blocks, block_rows, block_cols, interface_maps, merge_maps
):
    local_rows = load_interior.shape[2]
    quarter = load_boundary.shape[2]
    joined = jnp.concatenate([load_interior, load_boundary], axis=2)
    joined = lax.all_to_all(joined, "sub", split_axis=1, concat_axis=0, tiled=True)
    interior = jnp.transpose(joined[:, 0, :local_rows])
    boundary = jnp.transpose(joined[:, 0, local_rows:])
    num_cases = interior.shape[1]
    block_count = cond_blocks.shape[1]
    block_size = BLK
    blocks = cond_blocks[0].reshape(block_count, block_size, block_size)
    groups = lax.axis_size("case")
    full_rows = quarter * groups
    position = lax.axis_index("case")
    local_cols = block_cols[0] - position * (local_rows // block_size)
    pieces = jnp.take(
        interior.reshape(local_rows // block_size, block_size, num_cases), local_cols, axis=0
    )
    products = jnp.einsum("krc,kcn->krn", blocks, pieces, precision=lax.Precision.HIGHEST)
    row_blocks = full_rows // block_size
    onehot = (block_rows[0][None, :] == jnp.arange(row_blocks, dtype=jnp.int32)[:, None]).astype(
        jnp.float32
    )
    partial_value = jnp.dot(
        onehot,
        products.reshape(block_count, block_size * num_cases),
        precision=lax.Precision.HIGHEST,
    )
    partial_value = partial_value.reshape(full_rows, num_cases)
    embedded = lax.dynamic_update_slice(
        jnp.zeros((full_rows, num_cases), jnp.float32), boundary, (position * quarter, 0)
    )
    contribution = embedded - partial_value
    leaf_share, current = case_allreduce(contribution, position)
    slot = lax.axis_index("sub")
    levels = lax.axis_size("sub").bit_length() - 1
    nodes = jnp.zeros((quarter, num_cases), jnp.float32)
    for level in range(1, levels + 1):
        half = 1 << level - 1
        maps = interface_maps[0, level - 1]
        last = level == levels
        if last:
            matrix = merge_maps[0, level - 1]
        else:
            matrix = lax.all_gather(merge_maps[0, level - 1], "case", axis=0, tiled=True)
        shared_rows = matrix.shape[1]
        upper = slot // half % 2 == 1
        if level == 1:
            other = from_partner(current, "sub", 0)
            stacked = jnp.concatenate([current, other], axis=0)

            def partner_index(index):
                return index + full_rows

        else:
            core = slot % 2
            rows_half = full_rows // 2
            piece = lax.dynamic_slice_in_dim(current, core * rows_half, rows_half, 0)
            got = from_partner(piece, "sub", level - 1)
            swapped = from_partner(got, "sub", 0)
            stacked = jnp.concatenate([current, got, swapped], axis=0)

            def partner_index(index):
                away = (index // rows_half != core).astype(index.dtype)
                return full_rows + index % rows_half + rows_half * away

        def left_index(index):
            return jnp.where(upper, partner_index(index), index)

        def right_index(index):
            return jnp.where(upper, index, partner_index(index))

        shared = jnp.take(stacked, left_index(maps[0, :shared_rows]), axis=0) + jnp.take(
            stacked, right_index(maps[1, :shared_rows]), axis=0
        )
        kept_index = jnp.concatenate(
            [left_index(maps[0, shared_rows:]), right_index(maps[1, shared_rows:])]
        )
        if last:
            kept_index = lax.dynamic_slice_in_dim(kept_index, position * quarter, quarter)
        parent = jnp.take(stacked, kept_index, axis=0) - jnp.dot(
            matrix, shared, precision=lax.Precision.HIGHEST
        )
        is_node = slot % (2 * half) == half
        if last:
            is_node = jnp.logical_or(is_node, slot == 0)
            own = parent
        else:
            own = lax.dynamic_slice_in_dim(parent, position * quarter, quarter, 0)
        nodes = jnp.where(is_node, own, nodes)
        current = parent
    return (leaf_share[None], nodes[None])


def solution(mesh):
    placed = (
        P("sub", None, "case"),
        P("sub", None, "case"),
        P("sub", "case", None),
        P("sub", "case"),
        P("sub", "case"),
        P("sub", None, None, None),
        P("sub", None, "case", None),
    )
    return jax.shard_map(
        on_device,
        mesh=mesh,
        in_specs=placed,
        out_specs=(P("sub", "case", None), P("sub", "case", None)),
        check_vma=False,
    )
```

```python
import jax
import jax.numpy as jnp
from jax import lax
from jax.sharding import PartitionSpec as P

BLK = 64


def from_partner(value, axis, distance):
    mask = 2**distance
    pairs = [(source, source ^ mask) for source in range(lax.axis_size(axis))]
    return lax.ppermute(value, axis, pairs)


def shifted(value, axis, shift):
    size = lax.axis_size(axis)
    pairs = [(source, (source + shift) % size) for source in range(size)]
    return lax.ppermute(value, axis, pairs)


def case_allreduce(value, position):
    groups = lax.axis_size("case")
    quarter = value.shape[0] // groups
    chunks = value.reshape(groups, quarter, value.shape[1])
    mine = chunks[position]
    for shift in range(1, groups):
        outgoing = chunks[(position + shift) % groups]
        mine = mine + shifted(outgoing, "case", shift)
    pieces = [mine] + [shifted(mine, "case", shift) for shift in range(1, groups)]
    stacked = jnp.stack(pieces)
    order = (position - jnp.arange(groups)) % groups
    full = jnp.take(stacked, order, axis=0).reshape(value.shape)
    return mine, full


def on_device(
    load_interior, load_boundary, cond_blocks, block_rows, block_cols, interface_maps, merge_maps
):
    local_rows = load_interior.shape[2]
    quarter = load_boundary.shape[2]
    joined = jnp.concatenate([load_interior, load_boundary], axis=2)
    joined = lax.all_to_all(joined, "sub", split_axis=1, concat_axis=0, tiled=True)
    interior = jnp.transpose(joined[:, 0, :local_rows])
    boundary = jnp.transpose(joined[:, 0, local_rows:])
    num_cases = interior.shape[1]
    block_count = cond_blocks.shape[1]
    block_size = BLK
    blocks = cond_blocks[0].reshape(block_count, block_size, block_size)
    groups = lax.axis_size("case")
    full_rows = quarter * groups
    position = lax.axis_index("case")
    local_cols = block_cols[0] - position * (local_rows // block_size)
    pieces = jnp.take(
        interior.reshape(local_rows // block_size, block_size, num_cases), local_cols, axis=0
    )
    products = jnp.einsum("krc,kcn->krn", blocks, pieces, precision=lax.Precision.HIGHEST)
    row_blocks = full_rows // block_size
    onehot = (block_rows[0][None, :] == jnp.arange(row_blocks, dtype=jnp.int32)[:, None]).astype(
        jnp.float32
    )
    partial_value = jnp.dot(
        onehot,
        products.reshape(block_count, block_size * num_cases),
        precision=lax.Precision.HIGHEST,
    )
    partial_value = partial_value.reshape(full_rows, num_cases)
    embedded = lax.dynamic_update_slice(
        jnp.zeros((full_rows, num_cases), jnp.float32), boundary, (position * quarter, 0)
    )
    contribution = embedded - partial_value
    leaf_share, current = case_allreduce(contribution, position)
    slot = lax.axis_index("sub")
    levels = lax.axis_size("sub").bit_length() - 1
    nodes = jnp.zeros((quarter, num_cases), jnp.float32)
    core = slot % 2
    rows_half = full_rows // 2
    turn = core * rows_half
    rest = None
    for level in range(1, levels + 1):
        half = 1 << level - 1
        maps = interface_maps[0, level - 1]
        last = level == levels
        if last:
            matrix = merge_maps[0, level - 1]
        else:
            matrix = lax.all_gather(merge_maps[0, level - 1], "case", axis=0, tiled=True)
        shared_rows = matrix.shape[1]
        upper = slot // half % 2 == 1
        if level == 1:
            other = from_partner(current, "sub", 0)
            stacked = jnp.concatenate([current, other], axis=0)

            def own_index(index):
                return index

        else:
            got = from_partner(current[:rows_half], "sub", level - 1)
            got, rest = lax.optimization_barrier((got, rest))
            swapped = from_partner(got, "sub", 0)
            stacked = jnp.concatenate([current, got, swapped], axis=0)

            def own_index(index):
                return jnp.bitwise_xor(index, turn)

        def left_index(index):
            return jnp.where(upper, own_index(index) + full_rows, own_index(index))

        def right_index(index):
            return jnp.where(upper, own_index(index), own_index(index) + full_rows)

        shared = jnp.take(stacked, left_index(maps[0, :shared_rows]), axis=0) + jnp.take(
            stacked, right_index(maps[1, :shared_rows]), axis=0
        )
        kept_index = jnp.concatenate(
            [left_index(maps[0, shared_rows:]), right_index(maps[1, shared_rows:])]
        )

        def rows_of(begin, count):
            index = lax.dynamic_slice_in_dim(kept_index, begin, count)
            if last:
                part = lax.dynamic_slice_in_dim(matrix, 0, count, 0)
            else:
                part = lax.dynamic_slice_in_dim(matrix, begin, count, 0)
            return jnp.take(stacked, index, axis=0) - jnp.dot(
                part, shared, precision=lax.Precision.HIGHEST
            )

        is_node = slot % (2 * half) == half
        if last:
            is_node = jnp.logical_or(is_node, slot == 0)
            own = rows_of(position * quarter, quarter)
        else:
            first = rows_of(turn, rows_half)
            second = rows_of(rows_half - turn, rows_half)
            current = jnp.concatenate([first, second], axis=0)
            rest = second
            own = lax.dynamic_slice_in_dim(
                current, jnp.bitwise_xor(position * quarter, turn), quarter, 0
            )
        nodes = jnp.where(is_node, own, nodes)
    return (leaf_share[None], nodes[None])


def solution(mesh):
    placed = (
        P("sub", None, "case"),
        P("sub", None, "case"),
        P("sub", "case", None),
        P("sub", "case"),
        P("sub", "case"),
        P("sub", None, None, None),
        P("sub", None, "case", None),
    )
    return jax.shard_map(
        on_device,
        mesh=mesh,
        in_specs=placed,
        out_specs=(P("sub", "case", None), P("sub", "case", None)),
        check_vma=False,
    )
```

```python
import jax
import jax.numpy as jnp
from jax import lax
from jax.sharding import PartitionSpec as P

BLK = 64


def from_partner(value, axis, distance):
    mask = 2**distance
    pairs = [(source, source ^ mask) for source in range(lax.axis_size(axis))]
    return lax.ppermute(value, axis, pairs)


def shifted(value, axis, shift):
    size = lax.axis_size(axis)
    pairs = [(source, (source + shift) % size) for source in range(size)]
    return lax.ppermute(value, axis, pairs)


def case_allreduce(value, position):
    groups = lax.axis_size("case")
    quarter = value.shape[0] // groups
    chunks = value.reshape(groups, quarter, value.shape[1])
    mine = chunks[position]
    for shift in range(1, groups):
        outgoing = chunks[(position + shift) % groups]
        mine = mine + shifted(outgoing, "case", shift)
    pieces = [mine] + [shifted(mine, "case", shift) for shift in range(1, groups)]
    stacked = jnp.stack(pieces)
    order = (position - jnp.arange(groups)) % groups
    full = jnp.take(stacked, order, axis=0).reshape(value.shape)
    return mine, full


def on_device(
    load_interior, load_boundary, cond_blocks, block_rows, block_cols, interface_maps, merge_maps
):
    local_rows = load_interior.shape[2]
    quarter = load_boundary.shape[2]
    joined = jnp.concatenate([load_interior, load_boundary], axis=2)
    joined = lax.all_to_all(joined, "sub", split_axis=1, concat_axis=0, tiled=True)
    interior = jnp.transpose(joined[:, 0, :local_rows])
    boundary = jnp.transpose(joined[:, 0, local_rows:])
    num_cases = interior.shape[1]
    block_count = cond_blocks.shape[1]
    block_size = BLK
    blocks = cond_blocks[0].reshape(block_count, block_size, block_size)
    groups = lax.axis_size("case")
    full_rows = quarter * groups
    position = lax.axis_index("case")
    local_cols = block_cols[0] - position * (local_rows // block_size)
    pieces = jnp.take(
        interior.reshape(local_rows // block_size, block_size, num_cases), local_cols, axis=0
    )
    products = jnp.einsum("krc,kcn->krn", blocks, pieces, precision=lax.Precision.HIGH)
    row_blocks = full_rows // block_size
    onehot = (block_rows[0][None, :] == jnp.arange(row_blocks, dtype=jnp.int32)[:, None]).astype(
        jnp.float32
    )
    partial_value = jnp.dot(
        onehot,
        products.reshape(block_count, block_size * num_cases),
        precision=lax.Precision.HIGH,
    )
    partial_value = partial_value.reshape(full_rows, num_cases)
    embedded = lax.dynamic_update_slice(
        jnp.zeros((full_rows, num_cases), jnp.float32), boundary, (position * quarter, 0)
    )
    contribution = embedded - partial_value
    leaf_share, current = case_allreduce(contribution, position)
    slot = lax.axis_index("sub")
    levels = lax.axis_size("sub").bit_length() - 1
    nodes = jnp.zeros((quarter, num_cases), jnp.float32)
    core = slot % 2
    rows_half = full_rows // 2
    turn = core * rows_half
    rest = None
    for level in range(1, levels + 1):
        half = 1 << level - 1
        maps = interface_maps[0, level - 1]
        last = level == levels
        if last:
            matrix = merge_maps[0, level - 1]
        else:
            matrix = lax.all_gather(merge_maps[0, level - 1], "case", axis=0, tiled=True)
        shared_rows = matrix.shape[1]
        upper = slot // half % 2 == 1
        if level == 1:
            other = from_partner(current, "sub", 0)
            stacked = jnp.concatenate([current, other], axis=0)

            def own_index(index):
                return index

        else:
            got = from_partner(current[:rows_half], "sub", level - 1)
            got, rest = lax.optimization_barrier((got, rest))
            swapped = from_partner(got, "sub", 0)
            stacked = jnp.concatenate([current, got, swapped], axis=0)

            def own_index(index):
                return jnp.bitwise_xor(index, turn)

        def left_index(index):
            return jnp.where(upper, own_index(index) + full_rows, own_index(index))

        def right_index(index):
            return jnp.where(upper, own_index(index), own_index(index) + full_rows)

        shared = jnp.take(stacked, left_index(maps[0, :shared_rows]), axis=0) + jnp.take(
            stacked, right_index(maps[1, :shared_rows]), axis=0
        )
        kept_index = jnp.concatenate(
            [left_index(maps[0, shared_rows:]), right_index(maps[1, shared_rows:])]
        )

        def rows_of(begin, count):
            index = lax.dynamic_slice_in_dim(kept_index, begin, count)
            if last:
                part = lax.dynamic_slice_in_dim(matrix, 0, count, 0)
            else:
                part = lax.dynamic_slice_in_dim(matrix, begin, count, 0)
            return jnp.take(stacked, index, axis=0) - jnp.dot(
                part, shared, precision=lax.Precision.HIGH
            )

        is_node = slot % (2 * half) == half
        if last:
            is_node = jnp.logical_or(is_node, slot == 0)
            own = rows_of(position * quarter, quarter)
        else:
            first = rows_of(turn, rows_half)
            second = rows_of(rows_half - turn, rows_half)
            current = jnp.concatenate([first, second], axis=0)
            rest = second
            own = lax.dynamic_slice_in_dim(
                current, jnp.bitwise_xor(position * quarter, turn), quarter, 0
            )
        nodes = jnp.where(is_node, own, nodes)
    return (leaf_share[None], nodes[None])


def solution(mesh):
    placed = (
        P("sub", None, "case"),
        P("sub", None, "case"),
        P("sub", "case", None),
        P("sub", "case"),
        P("sub", "case"),
        P("sub", None, None, None),
        P("sub", None, "case", None),
    )
    return jax.shard_map(
        on_device,
        mesh=mesh,
        in_specs=placed,
        out_specs=(P("sub", "case", None), P("sub", "case", None)),
        check_vma=False,
    )
```

```python
import jax
import jax.numpy as jnp
from jax import lax
from jax.sharding import PartitionSpec as P

BLK = 64


def from_partner(value, axis, distance):
    mask = 2**distance
    pairs = [(source, source ^ mask) for source in range(lax.axis_size(axis))]
    return lax.ppermute(value, axis, pairs)


def to_row_quarters(value):
    return lax.all_to_all(value, "case", split_axis=0, concat_axis=1, tiled=True)


def on_device(
    load_interior, load_boundary, cond_blocks, block_rows, block_cols, interface_maps, merge_maps
):
    groups = lax.axis_size("case")
    local_rows = load_interior.shape[2]
    quarter = load_boundary.shape[2]
    full_rows = quarter * groups
    interior_rows = local_rows * groups
    block_size = BLK
    blocks = lax.all_gather(cond_blocks[0], "case", axis=0, tiled=True)
    rows_of_blocks = lax.all_gather(block_rows[0], "case", axis=0, tiled=True)
    cols_of_blocks = lax.all_gather(block_cols[0], "case", axis=0, tiled=True)
    block_count = blocks.shape[0]
    blocks = blocks.reshape(block_count, block_size, block_size)

    joined = jnp.concatenate([load_interior, load_boundary], axis=2)
    joined = lax.all_to_all(joined, "sub", split_axis=1, concat_axis=0, tiled=True)[:, 0, :]
    joined = lax.all_to_all(joined, "case", split_axis=0, concat_axis=1, tiled=True)
    num_cases = joined.shape[0]
    parts = joined.reshape(num_cases, groups, local_rows + quarter)
    interior = jnp.transpose(parts[:, :, :local_rows].reshape(num_cases, interior_rows))
    boundary = jnp.transpose(parts[:, :, local_rows:].reshape(num_cases, full_rows))

    pieces = jnp.take(
        interior.reshape(interior_rows // block_size, block_size, num_cases),
        cols_of_blocks,
        axis=0,
    )
    products = jnp.einsum("krc,kcn->krn", blocks, pieces, precision=lax.Precision.HIGH)
    row_blocks = full_rows // block_size
    onehot = (rows_of_blocks[None, :] == jnp.arange(row_blocks, dtype=jnp.int32)[:, None]).astype(
        jnp.float32
    )
    summed = jnp.dot(
        onehot,
        products.reshape(block_count, block_size * num_cases),
        precision=lax.Precision.HIGH,
    )
    leaf = boundary - summed.reshape(full_rows, num_cases)
    leaf_share = to_row_quarters(leaf)

    slot = lax.axis_index("sub")
    levels = lax.axis_size("sub").bit_length() - 1
    current = leaf
    nodes = jnp.zeros_like(leaf)
    for level in range(1, levels + 1):
        half = 1 << level - 1
        maps = interface_maps[0, level - 1]
        matrix = lax.all_gather(merge_maps[0, level - 1], "case", axis=0, tiled=True)
        shared_rows = matrix.shape[1]
        upper = slot // half % 2 == 1
        other = from_partner(current, "sub", level - 1)
        stacked = jnp.concatenate([current, other], axis=0)

        def left_index(index):
            return jnp.where(upper, index + full_rows, index)

        def right_index(index):
            return jnp.where(upper, index, index + full_rows)

        shared = jnp.take(stacked, left_index(maps[0, :shared_rows]), axis=0) + jnp.take(
            stacked, right_index(maps[1, :shared_rows]), axis=0
        )
        kept_index = jnp.concatenate(
            [left_index(maps[0, shared_rows:]), right_index(maps[1, shared_rows:])]
        )
        parent = jnp.take(stacked, kept_index, axis=0) - jnp.dot(
            matrix, shared, precision=lax.Precision.HIGH
        )
        is_node = slot % (2 * half) == half
        if level == levels:
            is_node = jnp.logical_or(is_node, slot == 0)
        nodes = jnp.where(is_node, parent, nodes)
        current = parent
    return (leaf_share[None], to_row_quarters(nodes)[None])


def solution(mesh):
    placed = (
        P("sub", None, "case"),
        P("sub", None, "case"),
        P("sub", "case", None),
        P("sub", "case"),
        P("sub", "case"),
        P("sub", None, None, None),
        P("sub", None, "case", None),
    )
    return jax.shard_map(
        on_device,
        mesh=mesh,
        in_specs=placed,
        out_specs=(P("sub", "case", None), P("sub", "case", None)),
        check_vma=False,
    )
```

```python
import jax
import jax.numpy as jnp
from jax import lax
from jax.sharding import PartitionSpec as P

BLK = 64


def from_partner(value, axis, distance):
    mask = 2**distance
    pairs = [(source, source ^ mask) for source in range(lax.axis_size(axis))]
    return lax.ppermute(value, axis, pairs)


def to_row_quarters(value):
    return lax.all_to_all(value, "case", split_axis=0, concat_axis=1, tiled=True)


def on_device(
    load_interior, load_boundary, cond_blocks, block_rows, block_cols, interface_maps, merge_maps
):
    groups = lax.axis_size("case")
    local_rows = load_interior.shape[2]
    quarter = load_boundary.shape[2]
    full_rows = quarter * groups
    interior_rows = local_rows * groups
    block_size = BLK
    blocks = lax.all_gather(cond_blocks[0], "case", axis=0, tiled=True)
    rows_of_blocks = lax.all_gather(block_rows[0], "case", axis=0, tiled=True)
    cols_of_blocks = lax.all_gather(block_cols[0], "case", axis=0, tiled=True)
    block_count = blocks.shape[0]
    blocks = blocks.reshape(block_count, block_size, block_size)

    joined = jnp.concatenate([load_interior, load_boundary], axis=2)
    joined = lax.all_to_all(joined, "sub", split_axis=1, concat_axis=0, tiled=True)[:, 0, :]
    joined = lax.all_to_all(joined, "case", split_axis=0, concat_axis=1, tiled=True)
    num_cases = joined.shape[0]
    parts = joined.reshape(num_cases, groups, local_rows + quarter)
    interior = jnp.transpose(parts[:, :, :local_rows].reshape(num_cases, interior_rows))
    boundary = jnp.transpose(parts[:, :, local_rows:].reshape(num_cases, full_rows))

    pieces = jnp.take(
        interior.reshape(interior_rows // block_size, block_size, num_cases),
        cols_of_blocks,
        axis=0,
    )
    products = jnp.einsum("krc,kcn->krn", blocks, pieces, precision=lax.Precision.HIGH)
    row_blocks = full_rows // block_size
    onehot = (rows_of_blocks[None, :] == jnp.arange(row_blocks, dtype=jnp.int32)[:, None]).astype(
        jnp.float32
    )
    summed = jnp.dot(
        onehot,
        products.reshape(block_count, block_size * num_cases),
        precision=lax.Precision.HIGH,
    )
    leaf = boundary - summed.reshape(full_rows, num_cases)
    leaf_share = to_row_quarters(leaf)

    slot = lax.axis_index("sub")
    levels = lax.axis_size("sub").bit_length() - 1
    current = leaf
    core = slot % 2
    nodes = jnp.zeros_like(leaf)
    for level in range(1, levels + 1):
        half = 1 << level - 1
        maps = interface_maps[0, level - 1]
        shared_rows = merge_maps.shape[3]
        width = shared_rows // 2
        begin = core * width
        mine = lax.dynamic_slice_in_dim(merge_maps[0, level - 1], begin, width, 1)
        mine = lax.all_gather(mine, "case", axis=0, tiled=True)
        theirs = from_partner(mine, "sub", 0)
        upper = slot // half % 2 == 1
        other = from_partner(current, "sub", level - 1)
        stacked = jnp.concatenate([current, other], axis=0)

        def left_index(index):
            return jnp.where(upper, index + full_rows, index)

        def right_index(index):
            return jnp.where(upper, index, index + full_rows)

        shared = jnp.take(stacked, left_index(maps[0, :shared_rows]), axis=0) + jnp.take(
            stacked, right_index(maps[1, :shared_rows]), axis=0
        )
        kept_index = jnp.concatenate(
            [left_index(maps[0, shared_rows:]), right_index(maps[1, shared_rows:])]
        )
        product = jnp.dot(
            mine,
            lax.dynamic_slice_in_dim(shared, begin, width, 0),
            precision=lax.Precision.HIGH,
        ) + jnp.dot(
            theirs,
            lax.dynamic_slice_in_dim(shared, width - begin, width, 0),
            precision=lax.Precision.HIGH,
        )
        parent = jnp.take(stacked, kept_index, axis=0) - product
        is_node = slot % (2 * half) == half
        if level == levels:
            is_node = jnp.logical_or(is_node, slot == 0)
        nodes = jnp.where(is_node, parent, nodes)
        current = parent
    return (leaf_share[None], to_row_quarters(nodes)[None])


def solution(mesh):
    placed = (
        P("sub", None, "case"),
        P("sub", None, "case"),
        P("sub", "case", None),
        P("sub", "case"),
        P("sub", "case"),
        P("sub", None, None, None),
        P("sub", None, "case", None),
    )
    return jax.shard_map(
        on_device,
        mesh=mesh,
        in_specs=placed,
        out_specs=(P("sub", "case", None), P("sub", "case", None)),
        check_vma=False,
    )
```

```python
import jax
import jax.numpy as jnp
from jax import lax
from jax.sharding import PartitionSpec as P

BLK = 64


def from_partner(value, axis, distance):
    mask = 2**distance
    pairs = [(source, source ^ mask) for source in range(lax.axis_size(axis))]
    return lax.ppermute(value, axis, pairs)


def shifted(value, axis, shift):
    size = lax.axis_size(axis)
    pairs = [(source, (source + shift) % size) for source in range(size)]
    return lax.ppermute(value, axis, pairs)


def case_allreduce(value, position):
    groups = lax.axis_size("case")
    quarter = value.shape[0] // groups
    chunks = value.reshape(groups, quarter, value.shape[1])
    received = lax.all_to_all(chunks, "case", split_axis=0, concat_axis=0)
    mine = received[0]
    for source in range(1, groups):
        mine = mine + received[source]
    copies = jnp.broadcast_to(mine[None], chunks.shape)
    full = lax.all_to_all(copies, "case", split_axis=0, concat_axis=0).reshape(value.shape)
    return mine, full


def on_device(
    load_interior, load_boundary, cond_blocks, block_rows, block_cols, interface_maps, merge_maps
):
    local_rows = load_interior.shape[2]
    quarter = load_boundary.shape[2]
    joined = jnp.concatenate([load_interior, load_boundary], axis=2)
    joined = lax.all_to_all(joined, "sub", split_axis=1, concat_axis=0, tiled=True)
    interior = jnp.transpose(joined[:, 0, :local_rows])
    boundary = jnp.transpose(joined[:, 0, local_rows:])
    num_cases = interior.shape[1]
    block_count = cond_blocks.shape[1]
    block_size = BLK
    blocks = cond_blocks[0].reshape(block_count, block_size, block_size)
    groups = lax.axis_size("case")
    full_rows = quarter * groups
    position = lax.axis_index("case")
    local_cols = block_cols[0] - position * (local_rows // block_size)
    pieces = jnp.take(
        interior.reshape(local_rows // block_size, block_size, num_cases), local_cols, axis=0
    )
    products = jnp.einsum("krc,kcn->krn", blocks, pieces, precision=lax.Precision.HIGH)
    row_blocks = full_rows // block_size
    onehot = (block_rows[0][None, :] == jnp.arange(row_blocks, dtype=jnp.int32)[:, None]).astype(
        jnp.float32
    )
    partial_value = jnp.dot(
        onehot,
        products.reshape(block_count, block_size * num_cases),
        precision=lax.Precision.HIGH,
    )
    partial_value = partial_value.reshape(full_rows, num_cases)
    embedded = lax.dynamic_update_slice(
        jnp.zeros((full_rows, num_cases), jnp.float32), boundary, (position * quarter, 0)
    )
    contribution = embedded - partial_value
    leaf_share, current = case_allreduce(contribution, position)
    slot = lax.axis_index("sub")
    levels = lax.axis_size("sub").bit_length() - 1
    nodes = jnp.zeros((quarter, num_cases), jnp.float32)
    core = slot % 2
    rows_half = full_rows // 2
    turn = core * rows_half
    rest = None
    for level in range(1, levels + 1):
        half = 1 << level - 1
        maps = interface_maps[0, level - 1]
        last = level == levels
        if last:
            matrix = merge_maps[0, level - 1]
        else:
            matrix = lax.all_gather(merge_maps[0, level - 1], "case", axis=0, tiled=True)
        shared_rows = matrix.shape[1]
        upper = slot // half % 2 == 1
        if level == 1:
            other = from_partner(current, "sub", 0)
            stacked = jnp.concatenate([current, other], axis=0)

            def own_index(index):
                return index

        else:
            got = from_partner(current[:rows_half], "sub", level - 1)
            got, rest = lax.optimization_barrier((got, rest))
            swapped = from_partner(got, "sub", 0)
            stacked = jnp.concatenate([current, got, swapped], axis=0)

            def own_index(index):
                return jnp.bitwise_xor(index, turn)

        def left_index(index):
            return jnp.where(upper, own_index(index) + full_rows, own_index(index))

        def right_index(index):
            return jnp.where(upper, own_index(index), own_index(index) + full_rows)

        shared = jnp.take(stacked, left_index(maps[0, :shared_rows]), axis=0) + jnp.take(
            stacked, right_index(maps[1, :shared_rows]), axis=0
        )
        kept_index = jnp.concatenate(
            [left_index(maps[0, shared_rows:]), right_index(maps[1, shared_rows:])]
        )

        def rows_of(begin, count):
            index = lax.dynamic_slice_in_dim(kept_index, begin, count)
            if last:
                part = lax.dynamic_slice_in_dim(matrix, 0, count, 0)
            else:
                part = lax.dynamic_slice_in_dim(matrix, begin, count, 0)
            return jnp.take(stacked, index, axis=0) - jnp.dot(
                part, shared, precision=lax.Precision.HIGH
            )

        is_node = slot % (2 * half) == half
        if last:
            is_node = jnp.logical_or(is_node, slot == 0)
            own = rows_of(position * quarter, quarter)
        else:
            first = rows_of(turn, rows_half)
            second = rows_of(rows_half - turn, rows_half)
            current = jnp.concatenate([first, second], axis=0)
            rest = second
            own = lax.dynamic_slice_in_dim(
                current, jnp.bitwise_xor(position * quarter, turn), quarter, 0
            )
        nodes = jnp.where(is_node, own, nodes)
    return (leaf_share[None], nodes[None])


def solution(mesh):
    placed = (
        P("sub", None, "case"),
        P("sub", None, "case"),
        P("sub", "case", None),
        P("sub", "case"),
        P("sub", "case"),
        P("sub", None, None, None),
        P("sub", None, "case", None),
    )
    return jax.shard_map(
        on_device,
        mesh=mesh,
        in_specs=placed,
        out_specs=(P("sub", "case", None), P("sub", "case", None)),
        check_vma=False,
    )
```

```python
import jax
import jax.numpy as jnp
from jax import lax
from jax.sharding import PartitionSpec as P

BLK = 64


def from_partner(value, axis, distance):
    mask = 2**distance
    pairs = [(source, source ^ mask) for source in range(lax.axis_size(axis))]
    return lax.ppermute(value, axis, pairs)


def shifted(value, axis, shift):
    size = lax.axis_size(axis)
    pairs = [(source, (source + shift) % size) for source in range(size)]
    return lax.ppermute(value, axis, pairs)


def case_allreduce(value, position):
    groups = lax.axis_size("case")
    quarter = value.shape[0] // groups
    chunks = value.reshape(groups, quarter, value.shape[1])
    received = lax.all_to_all(chunks, "case", split_axis=0, concat_axis=0)
    mine = received[0]
    for source in range(1, groups):
        mine = mine + received[source]
    copies = jnp.broadcast_to(mine[None], chunks.shape)
    full = lax.all_to_all(copies, "case", split_axis=0, concat_axis=0).reshape(value.shape)
    return mine, full


def on_device(
    load_interior, load_boundary, cond_blocks, block_rows, block_cols, interface_maps, merge_maps
):
    local_rows = load_interior.shape[2]
    quarter = load_boundary.shape[2]
    joined = jnp.concatenate([load_interior, load_boundary], axis=2)
    joined = lax.all_to_all(joined, "sub", split_axis=1, concat_axis=0, tiled=True)
    interior = jnp.transpose(joined[:, 0, :local_rows])
    boundary = jnp.transpose(joined[:, 0, local_rows:])
    num_cases = interior.shape[1]
    block_count = cond_blocks.shape[1]
    block_size = BLK
    blocks = cond_blocks[0].reshape(block_count, block_size, block_size)
    groups = lax.axis_size("case")
    full_rows = quarter * groups
    position = lax.axis_index("case")
    local_cols = block_cols[0] - position * (local_rows // block_size)
    pieces = jnp.take(
        interior.reshape(local_rows // block_size, block_size, num_cases), local_cols, axis=0
    )
    products = jnp.einsum("krc,kcn->krn", blocks, pieces, precision=lax.Precision.HIGH)
    row_blocks = full_rows // block_size
    onehot = (block_rows[0][None, :] == jnp.arange(row_blocks, dtype=jnp.int32)[:, None]).astype(
        jnp.float32
    )
    partial_value = jnp.dot(
        onehot,
        products.reshape(block_count, block_size * num_cases),
        precision=lax.Precision.HIGH,
    )
    partial_value = partial_value.reshape(full_rows, num_cases)
    embedded = lax.dynamic_update_slice(
        jnp.zeros((full_rows, num_cases), jnp.float32), boundary, (position * quarter, 0)
    )
    contribution = embedded - partial_value
    leaf_share, current = case_allreduce(contribution, position)
    slot = lax.axis_index("sub")
    levels = lax.axis_size("sub").bit_length() - 1
    nodes = jnp.zeros((quarter, num_cases), jnp.float32)
    core = slot % 2
    rows_half = full_rows // 2
    turn = core * rows_half
    rest = None
    for level in range(1, levels + 1):
        half = 1 << level - 1
        maps = interface_maps[0, level - 1]
        last = level == levels
        if last:
            matrix = merge_maps[0, level - 1]
        else:
            matrix = lax.all_gather(merge_maps[0, level - 1], "case", axis=0, tiled=True)
        shared_rows = matrix.shape[1]
        upper = slot // half % 2 == 1
        if level == 1:
            other = from_partner(current, "sub", 0)
            stacked = jnp.concatenate([current, other], axis=0)

            def own_index(index):
                return index

        else:
            got = from_partner(current[:rows_half], "sub", level - 1)
            got, rest = lax.optimization_barrier((got, rest))
            swapped = from_partner(got, "sub", 0)
            stacked = jnp.concatenate([current, got, swapped], axis=0)

            def own_index(index):
                return jnp.bitwise_xor(index, turn)

        def left_index(index):
            return jnp.where(upper, own_index(index) + full_rows, own_index(index))

        def right_index(index):
            return jnp.where(upper, own_index(index), own_index(index) + full_rows)

        kept_index = jnp.concatenate(
            [left_index(maps[0, shared_rows:]), right_index(maps[1, shared_rows:])]
        )
        if last:
            first_begin, first_count = position * quarter, quarter
        else:
            first_begin, first_count = turn, rows_half
        picked = jnp.take(
            stacked,
            jnp.concatenate(
                [
                    left_index(maps[0, :shared_rows]),
                    right_index(maps[1, :shared_rows]),
                    lax.dynamic_slice_in_dim(kept_index, first_begin, first_count),
                ]
            ),
            axis=0,
            mode="clip",
        )
        shared = picked[:shared_rows] + picked[shared_rows : 2 * shared_rows]

        def rows_of(begin, count, kept=None):
            if kept is None:
                index = lax.dynamic_slice_in_dim(kept_index, begin, count)
                kept = jnp.take(stacked, index, axis=0, mode="clip")
            if last:
                part = lax.dynamic_slice_in_dim(matrix, 0, count, 0)
            else:
                part = lax.dynamic_slice_in_dim(matrix, begin, count, 0)
            return kept - jnp.dot(part, shared, precision=lax.Precision.HIGH)

        first_kept = picked[2 * shared_rows :]

        is_node = slot % (2 * half) == half
        if last:
            is_node = jnp.logical_or(is_node, slot == 0)
            own = rows_of(first_begin, first_count, first_kept)
        else:
            first = rows_of(first_begin, first_count, first_kept)
            second = rows_of(rows_half - turn, rows_half)
            current = jnp.concatenate([first, second], axis=0)
            rest = second
            own = lax.dynamic_slice_in_dim(
                current, jnp.bitwise_xor(position * quarter, turn), quarter, 0
            )
        nodes = jnp.where(is_node, own, nodes)
    return (leaf_share[None], nodes[None])


def solution(mesh):
    placed = (
        P("sub", None, "case"),
        P("sub", None, "case"),
        P("sub", "case", None),
        P("sub", "case"),
        P("sub", "case"),
        P("sub", None, None, None),
        P("sub", None, "case", None),
    )
    return jax.shard_map(
        on_device,
        mesh=mesh,
        in_specs=placed,
        out_specs=(P("sub", "case", None), P("sub", "case", None)),
        check_vma=False,
    )
```

```python
import jax
import jax.numpy as jnp
from jax import lax
from jax.sharding import PartitionSpec as P

BLK = 64


def from_partner(value, axis, distance):
    mask = 2**distance
    pairs = [(source, source ^ mask) for source in range(lax.axis_size(axis))]
    return lax.ppermute(value, axis, pairs)


def shifted(value, axis, shift):
    size = lax.axis_size(axis)
    pairs = [(source, (source + shift) % size) for source in range(size)]
    return lax.ppermute(value, axis, pairs)


def case_allreduce(value, position):
    groups = lax.axis_size("case")
    quarter = value.shape[0] // groups
    chunks = value.reshape(groups, quarter, value.shape[1])
    received = lax.all_to_all(chunks, "case", split_axis=0, concat_axis=0)
    mine = received[0]
    for source in range(1, groups):
        mine = mine + received[source]
    copies = jnp.broadcast_to(mine[None], chunks.shape)
    full = lax.all_to_all(copies, "case", split_axis=0, concat_axis=0).reshape(value.shape)
    return mine, full


def on_device(
    load_interior, load_boundary, cond_blocks, block_rows, block_cols, interface_maps, merge_maps
):
    local_rows = load_interior.shape[2]
    quarter = load_boundary.shape[2]
    joined = jnp.concatenate([load_interior, load_boundary], axis=2)
    joined = lax.all_to_all(joined, "sub", split_axis=1, concat_axis=0, tiled=True)
    interior = jnp.transpose(joined[:, 0, :local_rows])
    boundary = jnp.transpose(joined[:, 0, local_rows:])
    num_cases = interior.shape[1]
    block_count = cond_blocks.shape[1]
    block_size = BLK
    blocks = cond_blocks[0].reshape(block_count, block_size, block_size)
    groups = lax.axis_size("case")
    full_rows = quarter * groups
    position = lax.axis_index("case")
    local_cols = block_cols[0] - position * (local_rows // block_size)
    pieces = jnp.take(
        interior.reshape(local_rows // block_size, block_size, num_cases), local_cols, axis=0
    )
    products = jnp.einsum("krc,kcn->krn", blocks, pieces, precision=lax.Precision.HIGH)
    row_blocks = full_rows // block_size
    onehot = (block_rows[0][None, :] == jnp.arange(row_blocks, dtype=jnp.int32)[:, None]).astype(
        jnp.float32
    )
    partial_value = jnp.dot(
        onehot,
        products.reshape(block_count, block_size * num_cases),
        precision=lax.Precision.HIGH,
    )
    partial_value = partial_value.reshape(full_rows, num_cases)
    embedded = lax.dynamic_update_slice(
        jnp.zeros((full_rows, num_cases), jnp.float32), boundary, (position * quarter, 0)
    )
    contribution = embedded - partial_value
    leaf_share, current = case_allreduce(contribution, position)
    slot = lax.axis_index("sub")
    levels = lax.axis_size("sub").bit_length() - 1
    nodes = jnp.zeros((quarter, num_cases), jnp.float32)
    core = slot % 2
    rows_half = full_rows // 2
    turn = core * rows_half
    rest = None
    for level in range(1, levels + 1):
        half = 1 << level - 1
        maps = interface_maps[0, level - 1]
        last = level == levels
        if last:
            matrix = merge_maps[0, level - 1]
        else:
            matrix = lax.all_gather(merge_maps[0, level - 1], "case", axis=0, tiled=True)
        shared_rows = matrix.shape[1]
        upper = slot // half % 2 == 1
        if level == 1:
            other = from_partner(current, "sub", 0)
            stacked = jnp.concatenate([current, other], axis=0)

            def own_index(index):
                return index

        else:
            if half in (8, 16):
                slice_rows = rows_half // groups
                piece = lax.dynamic_slice_in_dim(first, position * slice_rows, slice_rows, 0)
                piece = from_partner(piece, "sub", level - 1)
                copies = jnp.broadcast_to(piece[None], (groups,) + piece.shape)
                got = lax.all_to_all(copies, "case", split_axis=0, concat_axis=0)
                got = got.reshape(rows_half, num_cases)
            else:
                got = from_partner(first, "sub", level - 1)
            got, rest = lax.optimization_barrier((got, rest))
            swapped = from_partner(got, "sub", 0)
            stacked = jnp.concatenate([first, rest, got, swapped], axis=0)

            def own_index(index):
                return jnp.bitwise_xor(index, turn)

        def left_index(index):
            return jnp.where(upper, own_index(index) + full_rows, own_index(index))

        def right_index(index):
            return jnp.where(upper, own_index(index), own_index(index) + full_rows)

        kept_index = jnp.concatenate(
            [left_index(maps[0, shared_rows:]), right_index(maps[1, shared_rows:])]
        )
        if last:
            first_begin, first_count = position * quarter, quarter
        else:
            first_begin, first_count = turn, rows_half
        picked = jnp.take(
            stacked,
            jnp.concatenate(
                [
                    left_index(maps[0, :shared_rows]),
                    right_index(maps[1, :shared_rows]),
                    lax.dynamic_slice_in_dim(kept_index, first_begin, first_count),
                ]
            ),
            axis=0,
            mode="clip",
        )
        shared = picked[:shared_rows] + picked[shared_rows : 2 * shared_rows]

        def rows_of(begin, count, kept=None):
            if kept is None:
                index = lax.dynamic_slice_in_dim(kept_index, begin, count)
                kept = jnp.take(stacked, index, axis=0, mode="clip")
            if last:
                part = lax.dynamic_slice_in_dim(matrix, 0, count, 0)
            else:
                part = lax.dynamic_slice_in_dim(matrix, begin, count, 0)
            return kept - jnp.dot(part, shared, precision=lax.Precision.HIGH)

        first_kept = picked[2 * shared_rows :]

        is_node = slot % (2 * half) == half
        if last:
            is_node = jnp.logical_or(is_node, slot == 0)
            own = rows_of(first_begin, first_count, first_kept)
        else:
            first = rows_of(first_begin, first_count, first_kept)
            second = rows_of(rows_half - turn, rows_half)
            current = jnp.concatenate([first, second], axis=0)
            rest = second
            own = lax.dynamic_slice_in_dim(
                current, jnp.bitwise_xor(position * quarter, turn), quarter, 0
            )
        nodes = jnp.where(is_node, own, nodes)
    return (leaf_share[None], nodes[None])


def solution(mesh):
    placed = (
        P("sub", None, "case"),
        P("sub", None, "case"),
        P("sub", "case", None),
        P("sub", "case"),
        P("sub", "case"),
        P("sub", None, None, None),
        P("sub", None, "case", None),
    )
    return jax.shard_map(
        on_device,
        mesh=mesh,
        in_specs=placed,
        out_specs=(P("sub", "case", None), P("sub", "case", None)),
        check_vma=False,
    )
```

```python
import jax
import jax.numpy as jnp
from jax import lax
from jax.sharding import PartitionSpec as P

BLK = 64


def from_partner(value, axis, distance):
    mask = 2**distance
    pairs = [(source, source ^ mask) for source in range(lax.axis_size(axis))]
    return lax.ppermute(value, axis, pairs)


def shifted(value, axis, shift):
    size = lax.axis_size(axis)
    pairs = [(source, (source + shift) % size) for source in range(size)]
    return lax.ppermute(value, axis, pairs)


def case_allreduce(value, position):
    groups = lax.axis_size("case")
    quarter = value.shape[0] // groups
    copies = jnp.broadcast_to(value[None], (groups,) + value.shape)
    received = lax.all_to_all(copies, "case", split_axis=0, concat_axis=0)
    full = received[0]
    for source in range(1, groups):
        full = full + received[source]
    mine = lax.dynamic_slice_in_dim(full, position * quarter, quarter, 0)
    return mine, full


def on_device(
    load_interior, load_boundary, cond_blocks, block_rows, block_cols, interface_maps, merge_maps
):
    local_rows = load_interior.shape[2]
    quarter = load_boundary.shape[2]
    joined = jnp.concatenate([load_interior, load_boundary], axis=2)
    joined = lax.all_to_all(joined, "sub", split_axis=1, concat_axis=0, tiled=True)
    interior = jnp.transpose(joined[:, 0, :local_rows])
    boundary = jnp.transpose(joined[:, 0, local_rows:])
    num_cases = interior.shape[1]
    block_count = cond_blocks.shape[1]
    block_size = BLK
    blocks = cond_blocks[0].reshape(block_count, block_size, block_size)
    groups = lax.axis_size("case")
    full_rows = quarter * groups
    position = lax.axis_index("case")
    local_cols = block_cols[0] - position * (local_rows // block_size)
    pieces = jnp.take(
        interior.reshape(local_rows // block_size, block_size, num_cases), local_cols, axis=0
    )
    products = jnp.einsum("krc,kcn->krn", blocks, pieces, precision=lax.Precision.HIGH)
    row_blocks = full_rows // block_size
    onehot = (block_rows[0][None, :] == jnp.arange(row_blocks, dtype=jnp.int32)[:, None]).astype(
        jnp.float32
    )
    partial_value = jnp.dot(
        onehot,
        products.reshape(block_count, block_size * num_cases),
        precision=lax.Precision.HIGH,
    )
    partial_value = partial_value.reshape(full_rows, num_cases)
    embedded = lax.dynamic_update_slice(
        jnp.zeros((full_rows, num_cases), jnp.float32), boundary, (position * quarter, 0)
    )
    contribution = embedded - partial_value
    leaf_share, current = case_allreduce(contribution, position)
    slot = lax.axis_index("sub")
    levels = lax.axis_size("sub").bit_length() - 1
    nodes = jnp.zeros((quarter, num_cases), jnp.float32)
    core = slot % 2
    rows_half = full_rows // 2
    turn = core * rows_half
    rest = None
    for level in range(1, levels + 1):
        half = 1 << level - 1
        maps = interface_maps[0, level - 1]
        last = level == levels
        if last:
            matrix = merge_maps[0, level - 1]
        else:
            matrix = lax.all_gather(merge_maps[0, level - 1], "case", axis=0, tiled=True)
        shared_rows = matrix.shape[1]
        upper = slot // half % 2 == 1
        if level == 1:
            other = from_partner(current, "sub", 0)
            stacked = jnp.concatenate([current, other], axis=0)

            def own_index(index):
                return index

        else:
            got = from_partner(current[:rows_half], "sub", level - 1)
            got, rest = lax.optimization_barrier((got, rest))
            swapped = from_partner(got, "sub", 0)
            stacked = jnp.concatenate([current, got, swapped], axis=0)

            def own_index(index):
                return jnp.bitwise_xor(index, turn)

        def left_index(index):
            return jnp.where(upper, own_index(index) + full_rows, own_index(index))

        def right_index(index):
            return jnp.where(upper, own_index(index), own_index(index) + full_rows)

        kept_index = jnp.concatenate(
            [left_index(maps[0, shared_rows:]), right_index(maps[1, shared_rows:])]
        )
        if last:
            first_begin, first_count = position * quarter, quarter
        else:
            first_begin, first_count = turn, rows_half
        picked = jnp.take(
            stacked,
            jnp.concatenate(
                [
                    left_index(maps[0, :shared_rows]),
                    right_index(maps[1, :shared_rows]),
                    lax.dynamic_slice_in_dim(kept_index, first_begin, first_count),
                ]
            ),
            axis=0,
            mode="clip",
        )
        shared = picked[:shared_rows] + picked[shared_rows : 2 * shared_rows]

        def rows_of(begin, count, kept=None):
            if kept is None:
                index = lax.dynamic_slice_in_dim(kept_index, begin, count)
                kept = jnp.take(stacked, index, axis=0, mode="clip")
            if last:
                part = lax.dynamic_slice_in_dim(matrix, 0, count, 0)
            else:
                part = lax.dynamic_slice_in_dim(matrix, begin, count, 0)
            return kept - jnp.dot(part, shared, precision=lax.Precision.HIGH)

        first_kept = picked[2 * shared_rows :]

        is_node = slot % (2 * half) == half
        if last:
            is_node = jnp.logical_or(is_node, slot == 0)
            own = rows_of(first_begin, first_count, first_kept)
        else:
            first = rows_of(first_begin, first_count, first_kept)
            second = rows_of(rows_half - turn, rows_half)
            current = jnp.concatenate([first, second], axis=0)
            rest = second
            own = lax.dynamic_slice_in_dim(
                current, jnp.bitwise_xor(position * quarter, turn), quarter, 0
            )
        nodes = jnp.where(is_node, own, nodes)
    return (leaf_share[None], nodes[None])


def solution(mesh):
    placed = (
        P("sub", None, "case"),
        P("sub", None, "case"),
        P("sub", "case", None),
        P("sub", "case"),
        P("sub", "case"),
        P("sub", None, None, None),
        P("sub", None, "case", None),
    )
    return jax.shard_map(
        on_device,
        mesh=mesh,
        in_specs=placed,
        out_specs=(P("sub", "case", None), P("sub", "case", None)),
        check_vma=False,
    )
```

```python
import jax
import jax.numpy as jnp
from jax import lax
from jax.sharding import PartitionSpec as P

BLK = 64


def from_partner(value, axis, distance):
    mask = 2**distance
    pairs = [(source, source ^ mask) for source in range(lax.axis_size(axis))]
    return lax.ppermute(value, axis, pairs)


def shifted(value, axis, shift):
    size = lax.axis_size(axis)
    pairs = [(source, (source + shift) % size) for source in range(size)]
    return lax.ppermute(value, axis, pairs)


def case_allreduce(value, position):
    groups = lax.axis_size("case")
    quarter = value.shape[0] // groups
    chunks = value.reshape(groups, quarter, value.shape[1])
    received = lax.all_to_all(chunks, "case", split_axis=0, concat_axis=0)
    mine = received[0]
    for source in range(1, groups):
        mine = mine + received[source]
    copies = jnp.broadcast_to(mine[None], chunks.shape)
    full = lax.all_to_all(copies, "case", split_axis=0, concat_axis=0).reshape(value.shape)
    return mine, full


def on_device(
    load_interior, load_boundary, cond_blocks, block_rows, block_cols, interface_maps, merge_maps
):
    local_rows = load_interior.shape[2]
    quarter = load_boundary.shape[2]
    joined = jnp.concatenate([load_interior, load_boundary], axis=2)
    joined = lax.all_to_all(joined, "sub", split_axis=1, concat_axis=0, tiled=True)
    early = 2
    joined, later_maps = lax.optimization_barrier((joined, merge_maps[0, early:]))
    interior = jnp.transpose(joined[:, 0, :local_rows])
    boundary = jnp.transpose(joined[:, 0, local_rows:])
    num_cases = interior.shape[1]
    block_count = cond_blocks.shape[1]
    block_size = BLK
    blocks = cond_blocks[0].reshape(block_count, block_size, block_size)
    groups = lax.axis_size("case")
    full_rows = quarter * groups
    position = lax.axis_index("case")
    local_cols = block_cols[0] - position * (local_rows // block_size)
    pieces = jnp.take(
        interior.reshape(local_rows // block_size, block_size, num_cases), local_cols, axis=0
    )
    products = jnp.einsum("krc,kcn->krn", blocks, pieces, precision=lax.Precision.HIGH)
    row_blocks = full_rows // block_size
    onehot = (block_rows[0][None, :] == jnp.arange(row_blocks, dtype=jnp.int32)[:, None]).astype(
        jnp.float32
    )
    partial_value = jnp.dot(
        onehot,
        products.reshape(block_count, block_size * num_cases),
        precision=lax.Precision.HIGH,
    )
    partial_value = partial_value.reshape(full_rows, num_cases)
    embedded = lax.dynamic_update_slice(
        jnp.zeros((full_rows, num_cases), jnp.float32), boundary, (position * quarter, 0)
    )
    contribution = embedded - partial_value
    leaf_share, current = case_allreduce(contribution, position)
    slot = lax.axis_index("sub")
    levels = lax.axis_size("sub").bit_length() - 1
    nodes = jnp.zeros((quarter, num_cases), jnp.float32)
    core = slot % 2
    rows_half = full_rows // 2
    turn = core * rows_half
    rest = None
    for level in range(1, levels + 1):
        half = 1 << level - 1
        maps = interface_maps[0, level - 1]
        last = level == levels
        if last:
            matrix = merge_maps[0, level - 1]
        else:
            source = merge_maps[0, level - 1] if level <= early else later_maps[level - 1 - early]
            matrix = lax.all_gather(source, "case", axis=0, tiled=True)
        shared_rows = matrix.shape[1]
        upper = slot // half % 2 == 1
        if level == 1:
            other = from_partner(current, "sub", 0)
            stacked = jnp.concatenate([current, other], axis=0)

            def own_index(index):
                return index

        else:
            got = from_partner(current[:rows_half], "sub", level - 1)
            got, rest = lax.optimization_barrier((got, rest))
            swapped = from_partner(got, "sub", 0)
            stacked = jnp.concatenate([current, got, swapped], axis=0)

            def own_index(index):
                return jnp.bitwise_xor(index, turn)

        def left_index(index):
            return jnp.where(upper, own_index(index) + full_rows, own_index(index))

        def right_index(index):
            return jnp.where(upper, own_index(index), own_index(index) + full_rows)

        kept_index = jnp.concatenate(
            [left_index(maps[0, shared_rows:]), right_index(maps[1, shared_rows:])]
        )
        if last:
            first_begin, first_count = position * quarter, quarter
        else:
            first_begin, first_count = turn, rows_half
        picked = jnp.take(
            stacked,
            jnp.concatenate(
                [
                    left_index(maps[0, :shared_rows]),
                    right_index(maps[1, :shared_rows]),
                    lax.dynamic_slice_in_dim(kept_index, first_begin, first_count),
                ]
            ),
            axis=0,
            mode="clip",
        )
        shared = picked[:shared_rows] + picked[shared_rows : 2 * shared_rows]

        def rows_of(begin, count, kept=None):
            if kept is None:
                index = lax.dynamic_slice_in_dim(kept_index, begin, count)
                kept = jnp.take(stacked, index, axis=0, mode="clip")
            if last:
                part = lax.dynamic_slice_in_dim(matrix, 0, count, 0)
            else:
                part = lax.dynamic_slice_in_dim(matrix, begin, count, 0)
            return kept - jnp.dot(part, shared, precision=lax.Precision.HIGH)

        first_kept = picked[2 * shared_rows :]

        is_node = slot % (2 * half) == half
        if last:
            is_node = jnp.logical_or(is_node, slot == 0)
            own = rows_of(first_begin, first_count, first_kept)
        else:
            first = rows_of(first_begin, first_count, first_kept)
            second = rows_of(rows_half - turn, rows_half)
            current = jnp.concatenate([first, second], axis=0)
            rest = second
            own = lax.dynamic_slice_in_dim(
                current, jnp.bitwise_xor(position * quarter, turn), quarter, 0
            )
        nodes = jnp.where(is_node, own, nodes)
    return (leaf_share[None], nodes[None])


def solution(mesh):
    placed = (
        P("sub", None, "case"),
        P("sub", None, "case"),
        P("sub", "case", None),
        P("sub", "case"),
        P("sub", "case"),
        P("sub", None, None, None),
        P("sub", None, "case", None),
    )
    return jax.shard_map(
        on_device,
        mesh=mesh,
        in_specs=placed,
        out_specs=(P("sub", "case", None), P("sub", "case", None)),
        check_vma=False,
    )
```

```python
import jax
import jax.numpy as jnp
from jax import lax
from jax.sharding import PartitionSpec as P

BLK = 64


def from_partner(value, axis, distance):
    mask = 2**distance
    pairs = [(source, source ^ mask) for source in range(lax.axis_size(axis))]
    return lax.ppermute(value, axis, pairs)


def shifted(value, axis, shift):
    size = lax.axis_size(axis)
    pairs = [(source, (source + shift) % size) for source in range(size)]
    return lax.ppermute(value, axis, pairs)


def case_allreduce(value, boundary):
    groups = lax.axis_size("case")
    quarter = value.shape[0] // groups
    chunks = value.reshape(groups, quarter, value.shape[1])
    received = lax.all_to_all(chunks, "case", split_axis=0, concat_axis=0)
    summed = received[0]
    for source in range(1, groups):
        summed = summed + received[source]
    mine = boundary - summed
    copies = jnp.broadcast_to(mine[None], chunks.shape)
    full = lax.all_to_all(copies, "case", split_axis=0, concat_axis=0).reshape(value.shape)
    return mine, full


def on_device(
    load_interior, load_boundary, cond_blocks, block_rows, block_cols, interface_maps, merge_maps
):
    local_rows = load_interior.shape[2]
    quarter = load_boundary.shape[2]
    joined = jnp.concatenate([load_interior, load_boundary], axis=2)
    joined = lax.all_to_all(joined, "sub", split_axis=1, concat_axis=0, tiled=True)
    early = 2
    joined, later_maps = lax.optimization_barrier((joined, merge_maps[0, early:]))
    interior = jnp.transpose(joined[:, 0, :local_rows])
    boundary = jnp.transpose(joined[:, 0, local_rows:])
    num_cases = interior.shape[1]
    block_count = cond_blocks.shape[1]
    block_size = BLK
    blocks = cond_blocks[0].reshape(block_count, block_size, block_size)
    groups = lax.axis_size("case")
    full_rows = quarter * groups
    position = lax.axis_index("case")
    local_cols = block_cols[0] - position * (local_rows // block_size)
    pieces = jnp.take(
        interior.reshape(local_rows // block_size, block_size, num_cases), local_cols, axis=0
    )
    products = jnp.einsum("krc,kcn->krn", blocks, pieces, precision=lax.Precision.HIGH)
    row_blocks = full_rows // block_size
    onehot = (block_rows[0][None, :] == jnp.arange(row_blocks, dtype=jnp.int32)[:, None]).astype(
        jnp.float32
    )
    partial_value = jnp.dot(
        onehot,
        products.reshape(block_count, block_size * num_cases),
        precision=lax.Precision.HIGH,
    )
    partial_value = partial_value.reshape(full_rows, num_cases)
    leaf_share, current = case_allreduce(partial_value, boundary)
    slot = lax.axis_index("sub")
    levels = lax.axis_size("sub").bit_length() - 1
    nodes = jnp.zeros((quarter, num_cases), jnp.float32)
    core = slot % 2
    rows_half = full_rows // 2
    turn = core * rows_half
    rest = None
    for level in range(1, levels + 1):
        half = 1 << level - 1
        maps = interface_maps[0, level - 1]
        last = level == levels
        if last:
            matrix = merge_maps[0, level - 1]
        else:
            source = merge_maps[0, level - 1] if level <= early else later_maps[level - 1 - early]
            matrix = lax.all_gather(source, "case", axis=0, tiled=True)
        shared_rows = matrix.shape[1]
        upper = slot // half % 2 == 1
        if level == 1:
            other = from_partner(current, "sub", 0)
            stacked = jnp.concatenate([current, other], axis=0)

            def own_index(index):
                return index

        else:
            got = from_partner(current[:rows_half], "sub", level - 1)
            got, rest = lax.optimization_barrier((got, rest))
            swapped = from_partner(got, "sub", 0)
            stacked = jnp.concatenate([current, got, swapped], axis=0)

            def own_index(index):
                return jnp.bitwise_xor(index, turn)

        def left_index(index):
            return jnp.where(upper, own_index(index) + full_rows, own_index(index))

        def right_index(index):
            return jnp.where(upper, own_index(index), own_index(index) + full_rows)

        kept_index = jnp.concatenate(
            [left_index(maps[0, shared_rows:]), right_index(maps[1, shared_rows:])]
        )
        if last:
            first_begin, first_count = position * quarter, quarter
        else:
            first_begin, first_count = turn, rows_half
        picked = jnp.take(
            stacked,
            jnp.concatenate(
                [
                    left_index(maps[0, :shared_rows]),
                    right_index(maps[1, :shared_rows]),
                    lax.dynamic_slice_in_dim(kept_index, first_begin, first_count),
                ]
            ),
            axis=0,
            mode="clip",
        )
        shared = picked[:shared_rows] + picked[shared_rows : 2 * shared_rows]

        def rows_of(begin, count, kept=None):
            if kept is None:
                index = lax.dynamic_slice_in_dim(kept_index, begin, count)
                kept = jnp.take(stacked, index, axis=0, mode="clip")
            if last:
                part = lax.dynamic_slice_in_dim(matrix, 0, count, 0)
            else:
                part = lax.dynamic_slice_in_dim(matrix, begin, count, 0)
            return kept - jnp.dot(part, shared, precision=lax.Precision.HIGH)

        first_kept = picked[2 * shared_rows :]

        is_node = slot % (2 * half) == half
        if last:
            is_node = jnp.logical_or(is_node, slot == 0)
            own = rows_of(first_begin, first_count, first_kept)
        else:
            first = rows_of(first_begin, first_count, first_kept)
            second = rows_of(rows_half - turn, rows_half)
            current = jnp.concatenate([first, second], axis=0)
            rest = second
            own = lax.dynamic_slice_in_dim(
                current, jnp.bitwise_xor(position * quarter, turn), quarter, 0
            )
        nodes = jnp.where(is_node, own, nodes)
    return (leaf_share[None], nodes[None])


def solution(mesh):
    placed = (
        P("sub", None, "case"),
        P("sub", None, "case"),
        P("sub", "case", None),
        P("sub", "case"),
        P("sub", "case"),
        P("sub", None, None, None),
        P("sub", None, "case", None),
    )
    return jax.shard_map(
        on_device,
        mesh=mesh,
        in_specs=placed,
        out_specs=(P("sub", "case", None), P("sub", "case", None)),
        check_vma=False,
    )
```

```python
import jax
import jax.numpy as jnp
from jax import lax
from jax.sharding import PartitionSpec as P

BLK = 64


def from_partner(value, axis, distance):
    mask = 2**distance
    pairs = [(source, source ^ mask) for source in range(lax.axis_size(axis))]
    return lax.ppermute(value, axis, pairs)


def shifted(value, axis, shift):
    size = lax.axis_size(axis)
    pairs = [(source, (source + shift) % size) for source in range(size)]
    return lax.ppermute(value, axis, pairs)


def case_allreduce(value, boundary):
    groups = lax.axis_size("case")
    quarter = value.shape[0] // groups
    chunks = value.reshape(groups, quarter, value.shape[1])
    received = lax.all_to_all(chunks, "case", split_axis=0, concat_axis=0)
    summed = received[0]
    for source in range(1, groups):
        summed = summed + received[source]
    mine = boundary - summed
    copies = jnp.broadcast_to(mine[None], chunks.shape)
    full = lax.all_to_all(copies, "case", split_axis=0, concat_axis=0).reshape(value.shape)
    return mine, full


def on_device(
    load_interior, load_boundary, cond_blocks, block_rows, block_cols, interface_maps, merge_maps
):
    local_rows = load_interior.shape[2]
    quarter = load_boundary.shape[2]
    joined = jnp.concatenate([load_interior, load_boundary], axis=2)
    joined = lax.all_to_all(joined, "sub", split_axis=1, concat_axis=0, tiled=True)
    early = 1
    joined, later_maps = lax.optimization_barrier((joined, merge_maps[0, early:]))
    interior = jnp.transpose(joined[:, 0, :local_rows])
    boundary = jnp.transpose(joined[:, 0, local_rows:])
    num_cases = interior.shape[1]
    block_count = cond_blocks.shape[1]
    block_size = BLK
    blocks = cond_blocks[0].reshape(block_count, block_size, block_size)
    groups = lax.axis_size("case")
    full_rows = quarter * groups
    position = lax.axis_index("case")
    local_cols = block_cols[0] - position * (local_rows // block_size)
    pieces = jnp.take(
        interior.reshape(local_rows // block_size, block_size, num_cases), local_cols, axis=0
    )
    products = jnp.einsum("krc,kcn->krn", blocks, pieces, precision=lax.Precision.HIGH)
    row_blocks = full_rows // block_size
    onehot = (block_rows[0][None, :] == jnp.arange(row_blocks, dtype=jnp.int32)[:, None]).astype(
        jnp.float32
    )
    partial_value = jnp.dot(
        onehot,
        products.reshape(block_count, block_size * num_cases),
        precision=lax.Precision.HIGH,
    )
    partial_value = partial_value.reshape(full_rows, num_cases)
    leaf_share, current = case_allreduce(partial_value, boundary)
    slot = lax.axis_index("sub")
    levels = lax.axis_size("sub").bit_length() - 1
    nodes = jnp.zeros((quarter, num_cases), jnp.float32)
    core = slot % 2
    rows_half = full_rows // 2
    turn = core * rows_half
    rest = None
    for level in range(1, levels + 1):
        half = 1 << level - 1
        maps = interface_maps[0, level - 1]
        last = level == levels
        if last:
            matrix = merge_maps[0, level - 1]
        else:
            source = merge_maps[0, level - 1] if level <= early else later_maps[level - 1 - early]
            matrix = lax.all_gather(source, "case", axis=0, tiled=True)
        shared_rows = matrix.shape[1]
        upper = slot // half % 2 == 1
        if level == 1:
            other = from_partner(current, "sub", 0)
            stacked = jnp.concatenate([current, other], axis=0)

            def own_index(index):
                return index

        else:
            got = from_partner(current[:rows_half], "sub", level - 1)
            got, rest = lax.optimization_barrier((got, rest))
            swapped = from_partner(got, "sub", 0)
            stacked = jnp.concatenate([current, got, swapped], axis=0)

            def own_index(index):
                return jnp.bitwise_xor(index, turn)

        def left_index(index):
            return jnp.where(upper, own_index(index) + full_rows, own_index(index))

        def right_index(index):
            return jnp.where(upper, own_index(index), own_index(index) + full_rows)

        kept_index = jnp.concatenate(
            [left_index(maps[0, shared_rows:]), right_index(maps[1, shared_rows:])]
        )
        if last:
            first_begin, first_count = position * quarter, quarter
        else:
            first_begin, first_count = turn, rows_half
        picked = jnp.take(
            stacked,
            jnp.concatenate(
                [
                    left_index(maps[0, :shared_rows]),
                    right_index(maps[1, :shared_rows]),
                    lax.dynamic_slice_in_dim(kept_index, first_begin, first_count),
                ]
            ),
            axis=0,
            mode="clip",
        )
        shared = picked[:shared_rows] + picked[shared_rows : 2 * shared_rows]

        def rows_of(begin, count, kept=None):
            if kept is None:
                index = lax.dynamic_slice_in_dim(kept_index, begin, count)
                kept = jnp.take(stacked, index, axis=0, mode="clip")
            if last:
                part = lax.dynamic_slice_in_dim(matrix, 0, count, 0)
            else:
                part = lax.dynamic_slice_in_dim(matrix, begin, count, 0)
            return kept - jnp.dot(part, shared, precision=lax.Precision.HIGH)

        first_kept = picked[2 * shared_rows :]

        is_node = slot % (2 * half) == half
        if last:
            is_node = jnp.logical_or(is_node, slot == 0)
            own = rows_of(first_begin, first_count, first_kept)
        else:
            first = rows_of(first_begin, first_count, first_kept)
            second = rows_of(rows_half - turn, rows_half)
            current = jnp.concatenate([first, second], axis=0)
            rest = second
            own = lax.dynamic_slice_in_dim(
                current, jnp.bitwise_xor(position * quarter, turn), quarter, 0
            )
        nodes = jnp.where(is_node, own, nodes)
    return (leaf_share[None], nodes[None])


def solution(mesh):
    placed = (
        P("sub", None, "case"),
        P("sub", None, "case"),
        P("sub", "case", None),
        P("sub", "case"),
        P("sub", "case"),
        P("sub", None, None, None),
        P("sub", None, "case", None),
    )
    return jax.shard_map(
        on_device,
        mesh=mesh,
        in_specs=placed,
        out_specs=(P("sub", "case", None), P("sub", "case", None)),
        check_vma=False,
    )
```

```python
import jax
import jax.numpy as jnp
from jax import lax
from jax.sharding import PartitionSpec as P

BLK = 64


def from_partner(value, axis, distance):
    mask = 2**distance
    pairs = [(source, source ^ mask) for source in range(lax.axis_size(axis))]
    return lax.ppermute(value, axis, pairs)


def shifted(value, axis, shift):
    size = lax.axis_size(axis)
    pairs = [(source, (source + shift) % size) for source in range(size)]
    return lax.ppermute(value, axis, pairs)


def case_allreduce(value, boundary):
    groups = lax.axis_size("case")
    quarter = value.shape[0] // groups
    chunks = value.reshape(groups, quarter, value.shape[1])
    received = lax.all_to_all(chunks, "case", split_axis=0, concat_axis=0)
    summed = received[0]
    for source in range(1, groups):
        summed = summed + received[source]
    mine = boundary - summed
    copies = jnp.broadcast_to(mine[None], chunks.shape)
    full = lax.all_to_all(copies, "case", split_axis=0, concat_axis=0).reshape(value.shape)
    return mine, full


def on_device(
    load_interior, load_boundary, cond_blocks, block_rows, block_cols, interface_maps, merge_maps
):
    local_rows = load_interior.shape[2]
    quarter = load_boundary.shape[2]
    joined = jnp.concatenate([load_interior, load_boundary], axis=2)
    joined = lax.all_to_all(joined, "sub", split_axis=1, concat_axis=0, tiled=True)
    early = 2
    joined, later_maps = lax.optimization_barrier((joined, merge_maps[0, early:]))
    interior = jnp.transpose(joined[:, 0, :local_rows])
    boundary = jnp.transpose(joined[:, 0, local_rows:])
    num_cases = interior.shape[1]
    block_count = cond_blocks.shape[1]
    block_size = BLK
    blocks = cond_blocks[0].reshape(block_count, block_size, block_size)
    groups = lax.axis_size("case")
    full_rows = quarter * groups
    position = lax.axis_index("case")
    local_cols = block_cols[0] - position * (local_rows // block_size)
    pieces = jnp.take(
        interior.reshape(local_rows // block_size, block_size, num_cases),
        local_cols,
        axis=0,
        mode="clip",
    )
    products = jnp.einsum("krc,kcn->krn", blocks, pieces, precision=lax.Precision.HIGH)
    row_blocks = full_rows // block_size
    onehot = (block_rows[0][None, :] == jnp.arange(row_blocks, dtype=jnp.int32)[:, None]).astype(
        jnp.float32
    )
    partial_value = jnp.dot(
        onehot,
        products.reshape(block_count, block_size * num_cases),
        precision=lax.Precision.HIGH,
    )
    partial_value = partial_value.reshape(full_rows, num_cases)
    leaf_share, current = case_allreduce(partial_value, boundary)
    slot = lax.axis_index("sub")
    levels = lax.axis_size("sub").bit_length() - 1
    nodes = jnp.zeros((quarter, num_cases), jnp.float32)
    core = slot % 2
    rows_half = full_rows // 2
    turn = core * rows_half
    rest = None
    for level in range(1, levels + 1):
        half = 1 << level - 1
        maps = interface_maps[0, level - 1]
        last = level == levels
        if last:
            matrix = merge_maps[0, level - 1]
        else:
            source = merge_maps[0, level - 1] if level <= early else later_maps[level - 1 - early]
            matrix = lax.all_gather(source, "case", axis=0, tiled=True)
        shared_rows = matrix.shape[1]
        upper = slot // half % 2 == 1
        if level == 1:
            other = from_partner(current, "sub", 0)
            stacked = jnp.concatenate([current, other], axis=0)

            def own_index(index):
                return index

        else:
            got = from_partner(current[:rows_half], "sub", level - 1)
            got, rest = lax.optimization_barrier((got, rest))
            swapped = from_partner(got, "sub", 0)
            stacked = jnp.concatenate([current, got, swapped], axis=0)

            def own_index(index):
                return jnp.bitwise_xor(index, turn)

        def left_index(index):
            return jnp.where(upper, own_index(index) + full_rows, own_index(index))

        def right_index(index):
            return jnp.where(upper, own_index(index), own_index(index) + full_rows)

        kept_index = jnp.concatenate(
            [left_index(maps[0, shared_rows:]), right_index(maps[1, shared_rows:])]
        )
        if last:
            first_begin, first_count = position * quarter, quarter
        else:
            first_begin, first_count = turn, rows_half
        picked = jnp.take(
            stacked,
            jnp.concatenate(
                [
                    left_index(maps[0, :shared_rows]),
                    right_index(maps[1, :shared_rows]),
                    lax.dynamic_slice_in_dim(kept_index, first_begin, first_count),
                ]
            ),
            axis=0,
            mode="clip",
        )
        shared = picked[:shared_rows] + picked[shared_rows : 2 * shared_rows]

        def rows_of(begin, count, kept=None):
            if kept is None:
                index = lax.dynamic_slice_in_dim(kept_index, begin, count)
                kept = jnp.take(stacked, index, axis=0, mode="clip")
            if last:
                part = lax.dynamic_slice_in_dim(matrix, 0, count, 0)
            else:
                part = lax.dynamic_slice_in_dim(matrix, begin, count, 0)
            return kept - jnp.dot(part, shared, precision=lax.Precision.HIGH)

        first_kept = picked[2 * shared_rows :]

        is_node = slot % (2 * half) == half
        if last:
            is_node = jnp.logical_or(is_node, slot == 0)
            own = rows_of(first_begin, first_count, first_kept)
        else:
            first = rows_of(first_begin, first_count, first_kept)
            second = rows_of(rows_half - turn, rows_half)
            current = jnp.concatenate([first, second], axis=0)
            rest = second
            own = lax.dynamic_slice_in_dim(
                current, jnp.bitwise_xor(position * quarter, turn), quarter, 0
            )
        nodes = jnp.where(is_node, own, nodes)
    return (leaf_share[None], nodes[None])


def solution(mesh):
    placed = (
        P("sub", None, "case"),
        P("sub", None, "case"),
        P("sub", "case", None),
        P("sub", "case"),
        P("sub", "case"),
        P("sub", None, None, None),
        P("sub", None, "case", None),
    )
    return jax.shard_map(
        on_device,
        mesh=mesh,
        in_specs=placed,
        out_specs=(P("sub", "case", None), P("sub", "case", None)),
        check_vma=False,
    )
```
